768 devices in a mesh: dp: 32 (over y, x), fsdp: 24 (over z, core).
Axes of the slice: x: 4, y: 8, z: 12, core: 2. Of those that a mesh axis runs over, the one named last changes fastest.
Arguments:
- waveform: bfloat16 [24576, 50], P(('dp', 'fsdp')), may hold values from -6 to 6
- destination: int32 [24576, 1], P(('dp', 'fsdp')), may hold values from 0 to 31; in each aligned block of 32 rows (0 to 31, 32 to 63, ...) at most 2 rows name the same one
- lengths: int32 [24576], P(('dp', 'fsdp')), may hold values from 20 to 50
- conv0_weight: bfloat16 [10, 512], replicated, may hold values from -2 to 2
- conv1_weight: bfloat16 [1536, 512], replicated, may hold values from -0.15625 to 0.15625
- norm_gain: float32 [3, 512], replicated, may hold values from 0.1 to 1.9
- norm_bias: float32 [3, 512], replicated, may hold values from -3 to 3
- proj_weight: bfloat16 [512, 1920], P(None, 'fsdp'), may hold values from -0.25 to 0.25
- proj_bias: bfloat16 [1920], P('fsdp'), may hold values from -3 to 3
- cotangent: bfloat16 [49152, 4, 1920], P(('dp', 'fsdp')), may hold values from -0.078125 to 0.078125
Outputs:
- features: bfloat16 [49152, 4, 1920], P(('dp', 'fsdp'))
- grad_proj_weight: bfloat16 [512, 1920], P(None, 'fsdp')
- grad_proj_bias: bfloat16 [1920], P('fsdp')
The draws below stay inside these ranges and needn't reach their ends.
Inputs may be any that keep to these rules, and one draw needn't show every extreme that they name: On each device no destination is named by more than 2 of its rows, and on some devices one destination is named by exactly 2 rows.
All inputs are finite; a program needn't handle non-finite values.
Results may differ from the reference program's by a relative error of at most 0.0064.
Values may be sent and summed in bfloat16 or wider, within the bound.
No kernel may reach another device: no remote copies, remote signals or barrier semaphores. Data moves between devices by JAX's collectives and lax.ppermute only.
A program may use at most 64 MiB of HBM per device.

```python
import math
import jax
import jax.numpy as jnp
import numpy as np
from jax import lax

D_CONV = 512
D_MODEL = 1920
FR = 4
ROWS_DEV = 32
CAP = 2
SAMP = 50
ROWS = 24576
SLOTS = 49152
N_DP = 32
N_FSDP = 24


def with_ends(drawn, own_key, smallest, high):
    dims = drawn.shape
    index_at = [jax.random.randint(jax.random.fold_in(own_key, axis), (), 0, dims[axis]) for axis in range(len(dims))]
    drawn = drawn.at[tuple(index_at)].set(smallest)
    longest = dims.index(max(dims))
    index_at[longest] = (index_at[longest] + 1) % dims[longest]
    return drawn.at[tuple(index_at)].set(high)


def strengthened(drawn, own_key, source, target, blocks, factor):
    owner, partner = [(jnp.arange(drawn.shape[dim]) // (drawn.shape[dim] // blocks)).reshape([-1 if axis == dim else 1 for axis in range(drawn.ndim)]) for dim in (source, target)]
    chosen = jax.random.permutation(own_key, blocks)[partner]
    strong = (owner == chosen) | (owner == (partner + blocks // 2) % blocks)
    return jnp.where(strong, factor * drawn, drawn)


def level_of(key, shape, pieces, low, largest):
    def one(axis_at, parts):
        draws = jax.random.uniform(jax.random.fold_in(jax.random.fold_in(key, 6), axis_at), (parts,), jnp.float32, low / len(pieces), largest / len(pieces))
        return jnp.repeat(jnp.exp(draws), shape[axis_at] // parts).reshape((-1,) + (1,) * (len(shape) - axis_at - 1))

    loudness = one(*pieces[0])
    for cut in pieces[1:]:
        loudness = loudness * one(*cut)
    return loudness


def routed_block(key, own, number, rows, number_of, top, most, skew):
    sequence = jax.random.permutation(key, number_of)
    heavy_load, usual = shares(number_of, rows * top, most, skew, True), shares(number_of, rows * top, most, skew, False)
    places = jnp.arange(number_of)

    def named(sizes, offset_by):
        used = int((sizes > 0).sum())
        fixed = max(1, used // 4)
        moved = fixed + (places - fixed + offset_by * (used - fixed)) % max(1, number_of - fixed)
        return jnp.zeros((number_of,), jnp.int32).at[sequence[jnp.where(places < fixed, places, moved)]].set(jnp.asarray(sizes, jnp.int32))

    sizes = jnp.where(number % 4 == 0, named(heavy_load, number // 4), named(usual, number - number // 4 - 1))
    mixed = jax.random.permutation(jax.random.fold_in(own, 3), number_of)
    donor, sink = mixed[0:number_of // 2 * 2:2], mixed[1:number_of // 2 * 2:2]
    margin = jnp.minimum(sizes[donor] - 1, most - sizes[sink]) // 2
    margin = jnp.where((donor == sequence[0]) | (sink == sequence[0]) | (sizes[sink] == 0), 0, jnp.maximum(margin, 0))
    moved = jax.random.randint(jax.random.fold_in(own, 4), (number_of // 2,), 0, 1 << 20) % (margin + 1)
    sizes = sizes.at[donor].add(-moved).at[sink].add(moved)
    members = jnp.searchsorted(jnp.cumsum(sizes), jnp.arange(rows * top), side="right").astype(jnp.int32)
    listing = members.reshape(top, rows).T
    listing = listing[jax.random.permutation(jax.random.fold_in(own, 1), rows)]
    offset_by = jax.random.randint(jax.random.fold_in(own, 2), (rows, 1), 0, top)
    return jnp.take_along_axis(listing, (jnp.arange(top)[None, :] + offset_by) % top, axis=1)


def shares(amount, total, reach, lean, full):
    weights = [(1 << 20) // math.isqrt(standing ** lean) + 1 for standing in range(1, amount + 1)]
    largest = reach if full else min(reach, max(-(-total // amount), total * weights[0] // sum(weights)))
    least = 1 if total - largest >= amount - 1 else 0
    counts, spare = [largest] + [least] * (amount - 1), total - largest - least * (amount - 1)
    while spare > 0:
        candidates = [i for i in range(1, amount) if counts[i] < largest] or [i for i in range(1, amount) if counts[i] < reach]
        whole, left = sum([weights[i] for i in candidates]), spare
        for i in candidates:
            more = min(reach - counts[i], max(1, left * weights[i] // whole), spare)
            counts[i] = counts[i] + more
            spare = spare - more
    return np.array(counts)


def scatter_about(own_key, dims, spread, bound, cuts=(), held_as=jnp.bfloat16):
    array = spread * jax.random.normal(own_key, dims, jnp.float32)
    if cuts:
        array = array * level_of(own_key, dims, cuts, -0.22, 0.18)
    return jnp.clip(array, -bound, bound).astype(held_as)


def gaussian_with(rng, shape, scale, limit, cuts, heavy, kind=jnp.bfloat16):
    result = scale * jax.random.normal(rng, shape, jnp.float32)
    if cuts:
        result = result * level_of(rng, shape, cuts, -0.22, 0.18)
    return jnp.clip(strengthened(result, jax.random.fold_in(rng, 3), *heavy), -limit, limit).astype(kind)


def setup_inputs(seed: int = 0) -> dict:
    seeds = jax.random.split(jax.random.key(seed), 11)
    waveform = scatter_about(seeds[0], (ROWS, SAMP), 1.0, 6.0, ((0, 768),))
    destination_keys = jax.random.split(jax.random.fold_in(seeds[1], 1), ROWS // ROWS_DEV)
    destination_turns = jax.random.permutation(jax.random.fold_in(seeds[1], 3), ROWS // ROWS_DEV)
    destination = jax.vmap(lambda own, number: routed_block(jax.random.fold_in(seeds[1], 2), own, number, ROWS_DEV, N_DP, 1, CAP, 2))(destination_keys, destination_turns).reshape((ROWS, 1))
    lengths = with_ends(jax.random.randint(seeds[2], (ROWS,), 20, SAMP + 1), jax.random.fold_in(seeds[2], 1), 20, SAMP).astype(jnp.int32)
    conv0_weight = scatter_about(seeds[3], (10, D_CONV), 10 ** -0.5, 2.0)
    conv1_weight = scatter_about(seeds[4], (3 * D_CONV, D_CONV), (3 * D_CONV) ** -0.5, 0.15625)
    norm_gain = jnp.clip(1.0 + 0.18 * jax.random.normal(seeds[5], (3, D_CONV), jnp.float32), 0.1, 1.9)
    norm_bias = scatter_about(seeds[6], (3, D_CONV), 0.5, 3.0, (), jnp.float32)
    proj_weight = scatter_about(seeds[7], (D_CONV, D_MODEL), D_CONV ** -0.5, 0.25, ((1, 24),))
    proj_bias = scatter_about(seeds[8], (D_MODEL,), 0.5, 3.0, ((0, 24),))
    cotangent = gaussian_with(seeds[9], (SLOTS, FR, D_MODEL), (ROWS * FR) ** -0.5, 0.078125, ((0, 768),), (0, 2, 384, 6.0))
    return dict(waveform=waveform, destination=destination, lengths=lengths, conv0_weight=conv0_weight, conv1_weight=conv1_weight, norm_gain=norm_gain, norm_bias=norm_bias, proj_weight=proj_weight, proj_bias=proj_bias, cotangent=cotangent)


def layer_norm(values, gain_vec, bias_vec):
    avg_value = lax.optimization_barrier(jnp.mean(values, axis=-1, keepdims=True))
    centred = values - avg_value
    variance = lax.optimization_barrier(jnp.mean(centred * centred, axis=-1, keepdims=True))
    return centred * lax.rsqrt(variance + 1e-05) * gain_vec + bias_vec

def encode(wave_rows, conv0_weight, conv1_weight, norm_gain, norm_bias):
    row_count = wave_rows.shape[0]
    frame_count = (wave_rows.shape[1] - 10) // 10
    sample_blocks = wave_rows.reshape(row_count, 2 * frame_count + 2, 5)
    sample_pairs = jnp.concatenate([sample_blocks[:, :-1], sample_blocks[:, 1:]], axis=2).reshape(-1, 10)
    first_conv = jnp.dot(sample_pairs, conv0_weight, preferred_element_type=jnp.float32)
    first_conv = jax.nn.gelu(layer_norm(first_conv, norm_gain[0], norm_bias[0]), approximate=False).astype(jnp.bfloat16)
    first_conv = first_conv.reshape(row_count, 2 * frame_count + 1, -1)
    conv_taps = jnp.concatenate([first_conv[:, 0:2 * frame_count:2], first_conv[:, 1:2 * frame_count + 1:2], first_conv[:, 2:2 * frame_count + 2:2]], axis=2)
    second_conv = jnp.dot(conv_taps.reshape(row_count * frame_count, -1), conv1_weight, preferred_element_type=jnp.float32)
    return jax.nn.gelu(layer_norm(second_conv, norm_gain[1], norm_bias[1]), approximate=False).astype(jnp.bfloat16)

def reference(waveform, destination, lengths, conv0_weight, conv1_weight, norm_gain, norm_bias, proj_weight, proj_bias, cotangent):
    devices = N_DP * N_FSDP
    row_order = jnp.arange(ROWS_DEV, dtype=jnp.int32)
    targets = destination.reshape(devices, ROWS_DEV)
    same_dest = targets[:, :, None] == targets[:, None, :]
    earlier_rows = row_order[None, :] < row_order[:, None]
    row_rank = lax.optimization_barrier(jnp.sum((same_dest & earlier_rows[None]).astype(jnp.int32), axis=2))
    device_ids = jnp.arange(devices, dtype=jnp.int32)[:, None]
    slot = ((targets * N_FSDP + device_ids % N_FSDP) * N_DP + device_ids // N_FSDP) * CAP + row_rank
    frame_ids = jnp.arange(FR, dtype=jnp.int32)

    def scan_step(totals, step_input):
        wave_rows, row_lengths, slot_index = step_input
        grad_weight, grad_bias, feature_buf = totals
        hidden = encode(wave_rows, conv0_weight, conv1_weight, norm_gain, norm_bias)
        normed = layer_norm(hidden.astype(jnp.float32), norm_gain[2], norm_bias[2]).astype(jnp.bfloat16)
        valid = (10 * frame_ids[None, :] + 20 <= row_lengths[:, None]).reshape(-1, 1)
        frame_mask = valid.astype(jnp.float32)
        projected = jnp.dot(normed, proj_weight, preferred_element_type=jnp.float32) + proj_bias.astype(jnp.float32)
        feats_rows = (projected * frame_mask).astype(jnp.bfloat16).reshape(ROWS_DEV, FR, D_MODEL)
        feature_buf = feature_buf.at[slot_index].set(feats_rows)
        cot_rows = cotangent[slot_index].reshape(ROWS_DEV * FR, D_MODEL)
        grad_out = jnp.where(valid, cot_rows, jnp.zeros_like(cot_rows))
        grad_weight = grad_weight + lax.dot_general(normed, grad_out, (((0,), (0,)), ((), ())), preferred_element_type=jnp.float32)
        grad_bias = grad_bias + lax.optimization_barrier(jnp.sum(grad_out.astype(jnp.float32), axis=0))
        return ((grad_weight, grad_bias, feature_buf), None)
    initial = (jnp.zeros((D_CONV, D_MODEL), jnp.float32), jnp.zeros((D_MODEL,), jnp.float32), jnp.zeros((SLOTS, FR, D_MODEL), cotangent.dtype))
    totals, unused = lax.scan(scan_step, initial, (waveform.reshape(devices, ROWS_DEV, SAMP), lengths.reshape(devices, ROWS_DEV), slot))
    return (totals[2], totals[0].astype(jnp.bfloat16), totals[1].astype(jnp.bfloat16))
```

```python
import jax
import jax.numpy as jnp
from jax import lax
from jax.sharding import PartitionSpec as P


def layer_norm(values, gain_vec, bias_vec):
    avg_value = jnp.mean(values, axis=-1, keepdims=True)
    centred = values - avg_value
    variance = jnp.mean(centred * centred, axis=-1, keepdims=True)
    return centred * lax.rsqrt(variance + 1e-05) * gain_vec + bias_vec


def encode(wave_rows, frame_count, conv0_weight, conv1_weight, norm_gain, norm_bias):
    row_count = wave_rows.shape[0]
    taps = 3
    span = 10 * frame_count
    sample_pairs = jnp.concatenate(
        [
            wave_rows[:, 5 * k : 5 * k + span].reshape(row_count * frame_count, 10)
            for k in range(taps)
        ],
        axis=0,
    )
    first_conv = jnp.dot(sample_pairs, conv0_weight, preferred_element_type=jnp.float32)
    first_conv = jax.nn.gelu(
        layer_norm(first_conv, norm_gain[0], norm_bias[0]), approximate=False
    ).astype(jnp.bfloat16)
    channels = conv0_weight.shape[1]
    first_conv = first_conv.reshape(taps, row_count * frame_count, channels)
    second_conv = jnp.einsum(
        "krc,kcd->rd",
        first_conv,
        conv1_weight.reshape(taps, channels, -1),
        preferred_element_type=jnp.float32,
    )
    return jax.nn.gelu(
        layer_norm(second_conv, norm_gain[1], norm_bias[1]), approximate=False
    ).astype(jnp.bfloat16)


def local(
    waveform,
    destination,
    lengths,
    conv0_weight,
    conv1_weight,
    norm_gain,
    norm_bias,
    proj_weight,
    proj_bias,
    cotangent,
):
    dp_size = lax.axis_size("dp")
    row_count, samples = waveform.shape
    slot_count = cotangent.shape[0]
    frame_count = cotangent.shape[1]
    d_conv = proj_weight.shape[0]
    slot_cap = slot_count // dp_size
    weight_and_bias = lax.all_gather(
        jnp.concatenate([proj_weight, proj_bias[None, :]], axis=0), "fsdp", axis=1, tiled=True
    )
    weights, biases = weight_and_bias[:d_conv], weight_and_bias[d_conv]
    targets = destination[:, 0]
    row_order = jnp.arange(row_count, dtype=jnp.int32)
    same_dest = targets[:, None] == targets[None, :]
    earlier_rows = row_order[None, :] < row_order[:, None]
    row_rank = jnp.sum((same_dest & earlier_rows).astype(jnp.int32), axis=1)
    position = targets * slot_cap + row_rank
    placing = position[None, :] == jnp.arange(slot_count, dtype=jnp.int32)[:, None]
    rows_ext = jnp.concatenate([waveform, lengths.astype(jnp.bfloat16)[:, None]], axis=1)
    slot_rows = jnp.dot(
        placing.astype(jnp.bfloat16), rows_ext, preferred_element_type=jnp.float32
    ).astype(jnp.bfloat16)
    got = lax.all_to_all(
        slot_rows.reshape(dp_size, slot_cap, -1), "dp", split_axis=0, concat_axis=0, tiled=True
    ).reshape(slot_count, -1)
    got_wave = got[:, :samples]
    got_length = got[:, samples].astype(jnp.float32)
    hidden = encode(got_wave, frame_count, conv0_weight, conv1_weight, norm_gain, norm_bias)
    normed = layer_norm(hidden.astype(jnp.float32), norm_gain[2], norm_bias[2]).astype(jnp.bfloat16)
    frame_ids = jnp.arange(frame_count, dtype=jnp.float32)
    valid = (10 * frame_ids[None, :] + 20 <= got_length[:, None]).reshape(-1, 1)
    frame_mask = valid.astype(jnp.float32)
    projected = jnp.dot(normed, weights, preferred_element_type=jnp.float32) + biases.astype(
        jnp.float32
    )
    features = (projected * frame_mask).astype(jnp.bfloat16).reshape(slot_count, frame_count, -1)
    cot_rows = cotangent.reshape(slot_count * frame_count, -1)
    grad_out = jnp.where(valid, cot_rows, jnp.zeros_like(cot_rows))
    normed_ext = jnp.concatenate([normed, jnp.ones((normed.shape[0], 1), normed.dtype)], axis=1)
    grad_term = lax.dot_general(
        normed_ext, grad_out, (((0,), (0,)), ((), ())), preferred_element_type=jnp.float32
    )
    part = lax.psum_scatter(grad_term, "fsdp", scatter_dimension=1, tiled=True)
    total = lax.reduce_precision(lax.psum(part, "dp"), exponent_bits=8, mantissa_bits=7)
    grad_weight, grad_bias = total[:d_conv], total[d_conv]
    return (features, grad_weight.astype(jnp.bfloat16), grad_bias.astype(jnp.bfloat16))


def solution(mesh):
    in_specs = (
        P(("dp", "fsdp"), None),
        P(("dp", "fsdp"), None),
        P(("dp", "fsdp")),
        P(),
        P(),
        P(),
        P(),
        P(None, "fsdp"),
        P("fsdp"),
        P(("dp", "fsdp"), None, None),
    )
    out_specs = (P(("dp", "fsdp"), None, None), P(None, "fsdp"), P("fsdp"))
    return jax.shard_map(local, mesh=mesh, in_specs=in_specs, out_specs=out_specs, check_vma=False)
```

```python
import jax
import jax.numpy as jnp
from jax import lax
from jax.sharding import PartitionSpec as P


def layer_norm(values, gain_vec, bias_vec):
    avg_value = jnp.mean(values, axis=-1, keepdims=True)
    centred = values - avg_value
    variance = jnp.mean(centred * centred, axis=-1, keepdims=True)
    return centred * lax.rsqrt(variance + 1e-05) * gain_vec + bias_vec


def encode(wave_rows, frame_count, conv0_weight, conv1_weight, norm_gain, norm_bias):
    row_count = wave_rows.shape[0]
    taps = 3
    span = 10 * frame_count
    sample_pairs = jnp.concatenate(
        [
            wave_rows[:, 5 * k : 5 * k + span].reshape(row_count * frame_count, 10)
            for k in range(taps)
        ],
        axis=0,
    )
    first_conv = jnp.dot(sample_pairs, conv0_weight, preferred_element_type=jnp.float32)
    first_conv = jax.nn.gelu(
        layer_norm(first_conv, norm_gain[0], norm_bias[0]), approximate=False
    ).astype(jnp.bfloat16)
    channels = conv0_weight.shape[1]
    first_conv = first_conv.reshape(taps, row_count * frame_count, channels)
    second_conv = jnp.einsum(
        "krc,kcd->rd",
        first_conv,
        conv1_weight.reshape(taps, channels, -1),
        preferred_element_type=jnp.float32,
    )
    return jax.nn.gelu(
        layer_norm(second_conv, norm_gain[1], norm_bias[1]), approximate=False
    ).astype(jnp.bfloat16)


def step(
    waveform,
    destination,
    lengths,
    conv0_weight,
    conv1_weight,
    norm_gain,
    norm_bias,
    proj_weight,
    proj_bias,
    cotangent,
):
    dp_size = lax.axis_size("dp")
    row_count, samples = waveform.shape
    slot_count = cotangent.shape[0]
    frame_count = cotangent.shape[1]
    d_conv = proj_weight.shape[0]
    slot_cap = slot_count // dp_size
    fsdp_size = lax.axis_size("fsdp")
    own_block = jnp.concatenate([proj_weight, proj_bias[None, :]], axis=0)
    blocks = lax.all_to_all(
        jnp.broadcast_to(own_block[None], (fsdp_size,) + own_block.shape),
        "fsdp",
        split_axis=0,
        concat_axis=0,
        tiled=True,
    )
    weights, biases = blocks[:, :d_conv], blocks[:, d_conv].reshape(-1)
    targets = destination[:, 0]
    row_order = jnp.arange(row_count, dtype=jnp.int32)
    same_dest = targets[:, None] == targets[None, :]
    earlier_rows = row_order[None, :] < row_order[:, None]
    row_rank = jnp.sum((same_dest & earlier_rows).astype(jnp.int32), axis=1)
    position = targets * slot_cap + row_rank
    placing = position[None, :] == jnp.arange(slot_count, dtype=jnp.int32)[:, None]
    rows_ext = jnp.concatenate([waveform, lengths.astype(jnp.bfloat16)[:, None]], axis=1)
    slot_rows = jnp.dot(
        placing.astype(jnp.bfloat16), rows_ext, preferred_element_type=jnp.float32
    ).astype(jnp.bfloat16)
    got = lax.all_to_all(
        slot_rows.reshape(dp_size, slot_cap, -1), "dp", split_axis=0, concat_axis=0, tiled=True
    ).reshape(slot_count, -1)
    got_wave = got[:, :samples]
    got_length = got[:, samples].astype(jnp.float32)
    hidden = encode(got_wave, frame_count, conv0_weight, conv1_weight, norm_gain, norm_bias)
    normed = layer_norm(hidden.astype(jnp.float32), norm_gain[2], norm_bias[2]).astype(jnp.bfloat16)
    frame_ids = jnp.arange(frame_count, dtype=jnp.float32)
    valid = (10 * frame_ids[None, :] + 20 <= got_length[:, None]).reshape(-1, 1)
    frame_mask = valid.astype(jnp.float32)
    projected = jnp.einsum(
        "rc,jcn->rjn", normed, weights, preferred_element_type=jnp.float32
    ).reshape(normed.shape[0], -1) + biases.astype(jnp.float32)
    features = (projected * frame_mask).astype(jnp.bfloat16).reshape(slot_count, frame_count, -1)
    cot_rows = cotangent.reshape(slot_count * frame_count, -1)
    grad_out = jnp.where(valid, cot_rows, jnp.zeros_like(cot_rows))
    normed_ext = jnp.concatenate([normed, jnp.ones((normed.shape[0], 1), normed.dtype)], axis=1)
    grad_term = lax.dot_general(
        normed_ext, grad_out, (((0,), (0,)), ((), ())), preferred_element_type=jnp.float32
    )
    part = lax.psum_scatter(grad_term, "fsdp", scatter_dimension=1, tiled=True)
    total = part
    bit = 1
    while bit < dp_size:
        total = total + lax.ppermute(total, "dp", [(i, i ^ bit) for i in range(dp_size)])
        bit *= 2
    grad_weight, grad_bias = total[:d_conv], total[d_conv]
    return (features, grad_weight.astype(jnp.bfloat16), grad_bias.astype(jnp.bfloat16))


def solution(mesh):
    in_specs = (
        P(("dp", "fsdp"), None),
        P(("dp", "fsdp"), None),
        P(("dp", "fsdp")),
        P(),
        P(),
        P(),
        P(),
        P(None, "fsdp"),
        P("fsdp"),
        P(("dp", "fsdp"), None, None),
    )
    out_specs = (P(("dp", "fsdp"), None, None), P(None, "fsdp"), P("fsdp"))
    return jax.shard_map(step, mesh=mesh, in_specs=in_specs, out_specs=out_specs, check_vma=False)
```

```python
import jax
import jax.numpy as jnp
from jax import lax
from jax.sharding import PartitionSpec as P


def layer_norm(values, gain_vec, bias_vec):
    avg_value = jnp.mean(values, axis=-1, keepdims=True)
    centred = values - avg_value
    variance = jnp.mean(centred * centred, axis=-1, keepdims=True)
    return centred * lax.rsqrt(variance + 1e-05) * gain_vec + bias_vec


def encode(wave_rows, frame_count, conv0_weight, conv1_weight, norm_gain, norm_bias):
    row_count = wave_rows.shape[0]
    taps = 3
    span = 10 * frame_count
    sample_pairs = jnp.concatenate(
        [
            wave_rows[:, 5 * k : 5 * k + span].reshape(row_count * frame_count, 10)
            for k in range(taps)
        ],
        axis=0,
    )
    first_conv = jnp.dot(sample_pairs, conv0_weight, preferred_element_type=jnp.float32)
    first_conv = jax.nn.gelu(
        layer_norm(first_conv, norm_gain[0], norm_bias[0]), approximate=False
    ).astype(jnp.bfloat16)
    channels = conv0_weight.shape[1]
    first_conv = first_conv.reshape(taps, row_count * frame_count, channels)
    second_conv = jnp.einsum(
        "krc,kcd->rd",
        first_conv,
        conv1_weight.reshape(taps, channels, -1),
        preferred_element_type=jnp.float32,
    )
    return jax.nn.gelu(
        layer_norm(second_conv, norm_gain[1], norm_bias[1]), approximate=False
    ).astype(jnp.bfloat16)


def step(
    waveform,
    destination,
    lengths,
    conv0_weight,
    conv1_weight,
    norm_gain,
    norm_bias,
    proj_weight,
    proj_bias,
    cotangent,
):
    dp_size = lax.axis_size("dp")
    row_count, samples = waveform.shape
    slot_count = cotangent.shape[0]
    frame_count = cotangent.shape[1]
    d_conv = proj_weight.shape[0]
    slot_cap = slot_count // dp_size
    targets = destination[:, 0]
    row_order = jnp.arange(row_count, dtype=jnp.int32)
    same_dest = targets[:, None] == targets[None, :]
    earlier_rows = row_order[None, :] < row_order[:, None]
    row_rank = jnp.sum((same_dest & earlier_rows).astype(jnp.int32), axis=1)
    position = targets * slot_cap + row_rank
    placing = position[None, :] == jnp.arange(slot_count, dtype=jnp.int32)[:, None]
    rows_ext = jnp.concatenate([waveform, lengths.astype(jnp.bfloat16)[:, None]], axis=1)
    slot_rows = jnp.dot(
        placing.astype(jnp.bfloat16), rows_ext, preferred_element_type=jnp.float32
    ).astype(jnp.bfloat16)
    got = lax.all_to_all(
        slot_rows.reshape(dp_size, slot_cap, -1), "dp", split_axis=0, concat_axis=0, tiled=True
    ).reshape(slot_count, -1)
    got_wave = got[:, :samples]
    got_length = got[:, samples].astype(jnp.float32)
    hidden = encode(got_wave, frame_count, conv0_weight, conv1_weight, norm_gain, norm_bias)
    normed = layer_norm(hidden.astype(jnp.float32), norm_gain[2], norm_bias[2]).astype(jnp.bfloat16)
    frame_ids = jnp.arange(frame_count, dtype=jnp.float32)
    valid = (10 * frame_ids[None, :] + 20 <= got_length[:, None]).reshape(-1, 1)
    frame_mask = valid.astype(jnp.float32)
    cot_rows = cotangent.reshape(slot_count * frame_count, -1)
    grad_out = jnp.where(valid, cot_rows, jnp.zeros_like(cot_rows))
    normed_ext = jnp.concatenate([normed, jnp.ones((normed.shape[0], 1), normed.dtype)], axis=1)
    grad_term = lax.dot_general(
        normed_ext, grad_out, (((0,), (0,)), ((), ())), preferred_element_type=jnp.float32
    )
    fsdp_size = lax.axis_size("fsdp")
    own_block = jnp.concatenate([proj_weight, proj_bias[None, :]], axis=0)
    own_block, grad_term = lax.optimization_barrier((own_block, grad_term))
    blocks = lax.all_to_all(
        jnp.broadcast_to(own_block[None], (fsdp_size,) + own_block.shape),
        "fsdp",
        split_axis=0,
        concat_axis=0,
        tiled=True,
    )
    weights, biases = blocks[:, :d_conv], blocks[:, d_conv].reshape(-1)
    part = lax.psum_scatter(grad_term, "fsdp", scatter_dimension=1, tiled=True)
    projected = jnp.einsum(
        "rc,jcn->rjn", normed, weights, preferred_element_type=jnp.float32
    ).reshape(normed.shape[0], -1) + biases.astype(jnp.float32)
    features = (projected * frame_mask).astype(jnp.bfloat16).reshape(slot_count, frame_count, -1)

    rows = part.shape[0]
    piece_rows = -(-rows // dp_size)
    padded = jnp.pad(part, ((0, piece_rows * dp_size - rows), (0, 0)))
    pieces = lax.all_to_all(
        padded.reshape(dp_size, piece_rows, -1), "dp", split_axis=0, concat_axis=0, tiled=True
    )
    reduced = jnp.sum(pieces, axis=0).astype(jnp.bfloat16)
    gathered = lax.all_to_all(
        jnp.broadcast_to(reduced[None], (dp_size,) + reduced.shape),
        "dp",
        split_axis=0,
        concat_axis=0,
        tiled=True,
    )
    total = gathered.reshape(piece_rows * dp_size, -1)[:rows]
    grad_weight, grad_bias = total[:d_conv], total[d_conv]
    return (features, grad_weight, grad_bias)


def solution(mesh):
    in_specs = (
        P(("dp", "fsdp"), None),
        P(("dp", "fsdp"), None),
        P(("dp", "fsdp")),
        P(),
        P(),
        P(),
        P(),
        P(None, "fsdp"),
        P("fsdp"),
        P(("dp", "fsdp"), None, None),
    )
    out_specs = (P(("dp", "fsdp"), None, None), P(None, "fsdp"), P("fsdp"))
    return jax.shard_map(step, mesh=mesh, in_specs=in_specs, out_specs=out_specs, check_vma=False)
```

```python
import jax
import jax.numpy as jnp
from jax import lax
from jax.sharding import PartitionSpec as P


def layer_norm(values, gain_vec, bias_vec):
    avg_value = jnp.mean(values, axis=-1, keepdims=True)
    centred = values - avg_value
    variance = jnp.mean(centred * centred, axis=-1, keepdims=True)
    return centred * lax.rsqrt(variance + 1e-05) * gain_vec + bias_vec


def encode(wave_rows, frame_count, conv0_weight, conv1_weight, norm_gain, norm_bias):
    row_count = wave_rows.shape[0]
    taps = 3
    span = 10 * frame_count
    sample_pairs = jnp.concatenate(
        [
            wave_rows[:, 5 * k : 5 * k + span].reshape(row_count * frame_count, 10)
            for k in range(taps)
        ],
        axis=0,
    )
    first_conv = jnp.dot(sample_pairs, conv0_weight, preferred_element_type=jnp.float32)
    first_conv = jax.nn.gelu(
        layer_norm(first_conv, norm_gain[0], norm_bias[0]), approximate=False
    ).astype(jnp.bfloat16)
    channels = conv0_weight.shape[1]
    first_conv = first_conv.reshape(taps, row_count * frame_count, channels)
    second_conv = jnp.einsum(
        "krc,kcd->rd",
        first_conv,
        conv1_weight.reshape(taps, channels, -1),
        preferred_element_type=jnp.float32,
    )
    return jax.nn.gelu(
        layer_norm(second_conv, norm_gain[1], norm_bias[1]), approximate=False
    ).astype(jnp.bfloat16)


def step(
    waveform,
    destination,
    lengths,
    conv0_weight,
    conv1_weight,
    norm_gain,
    norm_bias,
    proj_weight,
    proj_bias,
    cotangent,
):
    dp_size = lax.axis_size("dp")
    row_count, samples = waveform.shape
    slot_count = cotangent.shape[0]
    frame_count = cotangent.shape[1]
    d_conv = proj_weight.shape[0]
    slot_cap = slot_count // dp_size
    targets = destination[:, 0]
    row_order = jnp.arange(row_count, dtype=jnp.int32)
    same_dest = targets[:, None] == targets[None, :]
    earlier_rows = row_order[None, :] < row_order[:, None]
    row_rank = jnp.sum((same_dest & earlier_rows).astype(jnp.int32), axis=1)
    position = targets * slot_cap + row_rank
    placing = position[None, :] == jnp.arange(slot_count, dtype=jnp.int32)[:, None]
    rows_ext = jnp.concatenate([waveform, lengths.astype(jnp.bfloat16)[:, None]], axis=1)
    slot_rows = jnp.dot(
        placing.astype(jnp.bfloat16), rows_ext, preferred_element_type=jnp.float32
    ).astype(jnp.bfloat16)
    got = lax.all_to_all(
        slot_rows.reshape(dp_size, slot_cap, -1), "dp", split_axis=0, concat_axis=0, tiled=True
    ).reshape(slot_count, -1)
    got_wave = got[:, :samples]
    got_length = got[:, samples].astype(jnp.float32)
    hidden = encode(got_wave, frame_count, conv0_weight, conv1_weight, norm_gain, norm_bias)
    normed = layer_norm(hidden.astype(jnp.float32), norm_gain[2], norm_bias[2]).astype(jnp.bfloat16)
    frame_ids = jnp.arange(frame_count, dtype=jnp.float32)
    valid = (10 * frame_ids[None, :] + 20 <= got_length[:, None]).reshape(-1, 1)
    frame_mask = valid.astype(jnp.float32)
    cot_rows = cotangent.reshape(slot_count * frame_count, -1)
    grad_out = jnp.where(valid, cot_rows, jnp.zeros_like(cot_rows))
    normed_ext = jnp.concatenate([normed, jnp.ones((normed.shape[0], 1), normed.dtype)], axis=1)
    grad_term = lax.dot_general(
        normed_ext, grad_out, (((0,), (0,)), ((), ())), preferred_element_type=jnp.float32
    )
    fsdp_size = lax.axis_size("z") * lax.axis_size("core")
    own_block = jnp.concatenate([proj_weight, proj_bias[None, :]], axis=0)
    blocks = lax.all_to_all(
        jnp.broadcast_to(own_block[None], (fsdp_size,) + own_block.shape),
        ("z", "core"),
        split_axis=0,
        concat_axis=0,
        tiled=True,
    )
    weights, biases = blocks[:, :d_conv], blocks[:, d_conv].reshape(-1)
    cores = lax.axis_size("core")
    core = lax.axis_index("core")
    by_core = grad_term.reshape(grad_term.shape[0], -1, cores, proj_weight.shape[1])
    mine = lax.dynamic_index_in_dim(by_core, core, axis=2, keepdims=False)
    other = lax.dynamic_index_in_dim(by_core, cores - 1 - core, axis=2, keepdims=False)
    pair_sum = mine + lax.ppermute(other, "core", [(0, 1), (1, 0)])
    part = lax.psum_scatter(pair_sum, "z", scatter_dimension=1, tiled=True)[:, 0]
    projected = jnp.einsum(
        "rc,jcn->rjn", normed, weights, preferred_element_type=jnp.float32
    ).reshape(normed.shape[0], -1) + biases.astype(jnp.float32)
    features = (projected * frame_mask).astype(jnp.bfloat16).reshape(slot_count, frame_count, -1)

    rows = part.shape[0]
    piece_rows = -(-rows // dp_size)
    padded = jnp.pad(part, ((0, piece_rows * dp_size - rows), (0, 0)))
    pieces = lax.all_to_all(
        padded.reshape(dp_size, piece_rows, -1), "dp", split_axis=0, concat_axis=0, tiled=True
    )
    reduced = jnp.sum(pieces, axis=0).astype(jnp.bfloat16)
    gathered = lax.all_to_all(
        jnp.broadcast_to(reduced[None], (dp_size,) + reduced.shape),
        "dp",
        split_axis=0,
        concat_axis=0,
        tiled=True,
    )
    total = gathered.reshape(piece_rows * dp_size, -1)[:rows]
    grad_weight, grad_bias = total[:d_conv], total[d_conv]
    return (features, grad_weight, grad_bias)


def solution(mesh):
    n_dp, n_fsdp = mesh.shape["dp"], mesh.shape["fsdp"]
    mesh = jax.sharding.Mesh(mesh.devices.reshape(n_dp, n_fsdp // 2, 2), ("dp", "z", "core"))
    rows = P(("dp", "z", "core"))
    in_specs = (
        P(("dp", "z", "core"), None),
        P(("dp", "z", "core"), None),
        rows,
        P(),
        P(),
        P(),
        P(),
        P(None, ("z", "core")),
        P(("z", "core")),
        P(("dp", "z", "core"), None, None),
    )
    out_specs = (P(("dp", "z", "core"), None, None), P(None, ("z", "core")), P(("z", "core")))
    return jax.shard_map(step, mesh=mesh, in_specs=in_specs, out_specs=out_specs, check_vma=False)
```

```python
import jax
import jax.numpy as jnp
from jax import lax
from jax.sharding import PartitionSpec as P


def layer_norm(values, gain_vec, bias_vec):
    avg_value = jnp.mean(values, axis=-1, keepdims=True)
    centred = values - avg_value
    variance = jnp.mean(centred * centred, axis=-1, keepdims=True)
    return centred * lax.rsqrt(variance + 1e-05) * gain_vec + bias_vec


def encode(wave_rows, frame_count, conv0_weight, conv1_weight, norm_gain, norm_bias):
    row_count = wave_rows.shape[0]
    taps = 3
    span = 10 * frame_count
    sample_pairs = jnp.concatenate(
        [
            wave_rows[:, 5 * k : 5 * k + span].reshape(row_count * frame_count, 10)
            for k in range(taps)
        ],
        axis=0,
    )
    first_conv = jnp.dot(sample_pairs, conv0_weight, preferred_element_type=jnp.float32)
    first_conv = jax.nn.gelu(
        layer_norm(first_conv, norm_gain[0], norm_bias[0]), approximate=False
    ).astype(jnp.bfloat16)
    channels = conv0_weight.shape[1]
    first_conv = first_conv.reshape(taps, row_count * frame_count, channels)
    second_conv = jnp.einsum(
        "krc,kcd->rd",
        first_conv,
        conv1_weight.reshape(taps, channels, -1),
        preferred_element_type=jnp.float32,
    )
    return jax.nn.gelu(
        layer_norm(second_conv, norm_gain[1], norm_bias[1]), approximate=False
    ).astype(jnp.bfloat16)


def step(
    waveform,
    destination,
    lengths,
    conv0_weight,
    conv1_weight,
    norm_gain,
    norm_bias,
    proj_weight,
    proj_bias,
    cotangent,
):
    dp_size = lax.axis_size("dp")
    row_count, samples = waveform.shape
    slot_count = cotangent.shape[0]
    frame_count = cotangent.shape[1]
    d_conv = proj_weight.shape[0]
    slot_cap = slot_count // dp_size
    targets = destination[:, 0]
    row_order = jnp.arange(row_count, dtype=jnp.int32)
    same_dest = targets[:, None] == targets[None, :]
    earlier_rows = row_order[None, :] < row_order[:, None]
    row_rank = jnp.sum((same_dest & earlier_rows).astype(jnp.int32), axis=1)
    position = targets * slot_cap + row_rank
    placing = position[None, :] == jnp.arange(slot_count, dtype=jnp.int32)[:, None]
    rows_ext = jnp.concatenate([waveform, lengths.astype(jnp.bfloat16)[:, None]], axis=1)
    slot_rows = jnp.dot(
        placing.astype(jnp.bfloat16), rows_ext, preferred_element_type=jnp.float32
    ).astype(jnp.bfloat16)
    got = lax.all_to_all(
        slot_rows.reshape(dp_size, slot_cap, -1), "dp", split_axis=0, concat_axis=0, tiled=True
    ).reshape(slot_count, -1)
    got_wave = got[:, :samples]
    got_length = got[:, samples].astype(jnp.float32)
    hidden = encode(got_wave, frame_count, conv0_weight, conv1_weight, norm_gain, norm_bias)
    normed = layer_norm(hidden.astype(jnp.float32), norm_gain[2], norm_bias[2]).astype(jnp.bfloat16)
    frame_ids = jnp.arange(frame_count, dtype=jnp.float32)
    valid = (10 * frame_ids[None, :] + 20 <= got_length[:, None]).reshape(-1, 1)
    frame_mask = valid.astype(jnp.float32)
    cot_rows = cotangent.reshape(slot_count * frame_count, -1)
    grad_out = jnp.where(valid, cot_rows, jnp.zeros_like(cot_rows))
    normed_ext = jnp.concatenate([normed, jnp.ones((normed.shape[0], 1), normed.dtype)], axis=1)
    grad_term = lax.dot_general(
        normed_ext, grad_out, (((0,), (0,)), ((), ())), preferred_element_type=jnp.float32
    )
    fsdp_size = lax.axis_size("z") * lax.axis_size("core")
    own_block = jnp.concatenate([proj_weight, proj_bias[None, :]], axis=0)
    cores = lax.axis_size("core")
    core = lax.axis_index("core")
    partner_block = lax.ppermute(own_block, "core", [(0, 1), (1, 0)])
    chip_blocks = jnp.where(
        core == 0, jnp.stack([own_block, partner_block]), jnp.stack([partner_block, own_block])
    )
    blocks = lax.all_to_all(
        jnp.broadcast_to(chip_blocks[None], (fsdp_size // cores,) + chip_blocks.shape),
        "z",
        split_axis=0,
        concat_axis=0,
        tiled=True,
    ).reshape((fsdp_size,) + own_block.shape)
    weights, biases = blocks[:, :d_conv], blocks[:, d_conv].reshape(-1)
    by_core = grad_term.reshape(grad_term.shape[0], -1, cores, proj_weight.shape[1])
    mine = lax.dynamic_index_in_dim(by_core, core, axis=2, keepdims=False)
    other = lax.dynamic_index_in_dim(by_core, cores - 1 - core, axis=2, keepdims=False)
    pair_sum = mine + lax.ppermute(other, "core", [(0, 1), (1, 0)])
    part = lax.psum_scatter(pair_sum, "z", scatter_dimension=1, tiled=True)[:, 0]
    projected = jnp.einsum(
        "rc,jcn->rjn", normed, weights, preferred_element_type=jnp.float32
    ).reshape(normed.shape[0], -1) + biases.astype(jnp.float32)
    features = (projected * frame_mask).astype(jnp.bfloat16).reshape(slot_count, frame_count, -1)

    rows = part.shape[0]
    piece_rows = -(-rows // dp_size)
    padded = jnp.pad(part, ((0, piece_rows * dp_size - rows), (0, 0)))
    pieces = lax.all_to_all(
        padded.reshape(dp_size, piece_rows, -1), "dp", split_axis=0, concat_axis=0, tiled=True
    )
    reduced = jnp.sum(pieces, axis=0).astype(jnp.bfloat16)
    gathered = lax.all_to_all(
        jnp.broadcast_to(reduced[None], (dp_size,) + reduced.shape),
        "dp",
        split_axis=0,
        concat_axis=0,
        tiled=True,
    )
    total = gathered.reshape(piece_rows * dp_size, -1)[:rows]
    grad_weight, grad_bias = total[:d_conv], total[d_conv]
    return (features, grad_weight, grad_bias)


def solution(mesh):
    n_dp, n_fsdp = mesh.shape["dp"], mesh.shape["fsdp"]
    mesh = jax.sharding.Mesh(mesh.devices.reshape(n_dp, n_fsdp // 2, 2), ("dp", "z", "core"))
    rows = P(("dp", "z", "core"))
    in_specs = (
        P(("dp", "z", "core"), None),
        P(("dp", "z", "core"), None),
        rows,
        P(),
        P(),
        P(),
        P(),
        P(None, ("z", "core")),
        P(("z", "core")),
        P(("dp", "z", "core"), None, None),
    )
    out_specs = (P(("dp", "z", "core"), None, None), P(None, ("z", "core")), P(("z", "core")))
    return jax.shard_map(step, mesh=mesh, in_specs=in_specs, out_specs=out_specs, check_vma=False)
```
